128 devices in a mesh: expert: 32 (over y, x, core), dp: 4 (over z).
Axes of the slice: x: 4, y: 4, z: 4, core: 2. Of those that a mesh axis runs over, the one named last changes fastest.
Arguments:
- tokens: bfloat16 [8192, 3584], P(('expert', 'dp')), may hold values from -6 to 6
- out_grad: bfloat16 [8192, 3584], P(('expert', 'dp')), may hold values from -6 to 6
- route_ids: int32 [8192, 8], P(('expert', 'dp')), may hold values from 0 to 31, all different within a row; in each aligned block of 64 rows (0 to 63, 64 to 127, ...) at most 20 rows name the same one
- route_logits: float32 [8192, 8], P(('expert', 'dp')), may hold values from -6 to 6
- gate_up: bfloat16 [32, 2, 3584, 1024], P('expert', None, None, 'dp'), may hold values from -0.09375 to 0.09375
- down: bfloat16 [32, 1024, 3584], P('expert', 'dp'), may hold values from -0.1875 to 0.1875
- moment1: bfloat16 [32, 1024, 3584], P('expert', 'dp'), may hold values from -8 to 8
- moment2: bfloat16 [32, 1024, 3584], P('expert', 'dp'), may hold values from 0.5 to 20
Outputs:
- token_grad: bfloat16 [8192, 3584], P(('expert', 'dp'))
- router_grad: float32 [8192, 8], P(('expert', 'dp'))
- new_down: bfloat16 [32, 1024, 3584], P('expert', 'dp')
- new_moment1: bfloat16 [32, 1024, 3584], P('expert', 'dp')
- new_moment2: bfloat16 [32, 1024, 3584], P('expert', 'dp')
The draws below stay inside these ranges and needn't reach their ends.
Inputs may be any that keep to these rules, and one draw needn't show every extreme that they name: `route_ids`: each row names 8 different experts. Within the 64 rows of one device no expert is named more than 20 times, and in every draw the rows of some device name some expert exactly 20 times.
All inputs are finite; a program needn't handle non-finite values.
Results may differ from the reference program's by a relative error of at most 0.012.
Values may be sent and summed in bfloat16 or wider, within the bound.
No kernel may reach another device: no remote copies, remote signals or barrier semaphores. Data moves between devices by JAX's collectives and lax.ppermute only.
A program may use at most 192 MiB of HBM per device.

```python
import math
import jax
import jax.numpy as jnp
import numpy as np
from jax import lax

D = 3584
FFW = 1024
TOP = 8
STEP = 10
TOK_DEV = 64
EXPERTS = 32
TOKENS = 8192
CAP = 20
N_EXPERT = 32
N_DP = 4


def levels(own_key, extent, shards, smallest, high):
    level, own = 1.0, jax.random.fold_in(own_key, 6)
    for dim, blocks in shards:
        steps = jnp.exp(jax.random.uniform(jax.random.fold_in(own, dim), (blocks,), jnp.float32, smallest / len(shards), high / len(shards)))
        level = level * jnp.repeat(steps, extent[dim] // blocks).reshape([-1 if axis == dim else 1 for axis in range(len(extent))])
    return level


def routed_block(rng, own, number, rows, count, top, bound, lean):
    ranking = jax.random.permutation(rng, count)
    crowded, usual = shares(count, rows * top, bound, lean, True), shares(count, rows * top, bound, lean, False)
    places = jnp.arange(count)

    def named(lengths, turn):
        used = int((lengths > 0).sum())
        fixed = max(1, used // 4)
        shifted = fixed + (places - fixed + turn * (used - fixed)) % max(1, count - fixed)
        return jnp.zeros((count,), jnp.int32).at[ranking[jnp.where(places < fixed, places, shifted)]].set(jnp.asarray(lengths, jnp.int32))

    lengths = jnp.where(number % 4 == 0, named(crowded, number // 4), named(usual, number - number // 4 - 1))
    mixed = jax.random.permutation(jax.random.fold_in(own, 3), count)
    donor, taker = mixed[0:count // 2 * 2:2], mixed[1:count // 2 * 2:2]
    room = jnp.minimum(lengths[donor] - 1, bound - lengths[taker]) // 2
    room = jnp.where((donor == ranking[0]) | (taker == ranking[0]) | (lengths[taker] == 0), 0, jnp.maximum(room, 0))
    shifted = jax.random.randint(jax.random.fold_in(own, 4), (count // 2,), 0, 1 << 20) % (room + 1)
    lengths = lengths.at[donor].add(-shifted).at[taker].add(shifted)
    members = jnp.searchsorted(jnp.cumsum(lengths), jnp.arange(rows * top), side="right").astype(jnp.int32)
    grid = members.reshape(top, rows).T
    grid = grid[jax.random.permutation(jax.random.fold_in(own, 1), rows)]
    turn = jax.random.randint(jax.random.fold_in(own, 2), (rows, 1), 0, top)
    return jnp.take_along_axis(grid, (jnp.arange(top)[None, :] + turn) % top, axis=1)


def shares(amount, total, limit, slope, full):
    weights = [(1 << 20) // math.isqrt(grade ** slope) + 1 for grade in range(1, amount + 1)]
    largest = limit if full else min(limit, max(-(-total // amount), total * weights[0] // sum(weights)))
    least = 1 if total - largest >= amount - 1 else 0
    holding, surplus = [largest] + [least] * (amount - 1), total - largest - least * (amount - 1)
    while surplus > 0:
        candidates = [i for i in range(1, amount) if holding[i] < largest] or [i for i in range(1, amount) if holding[i] < limit]
        pool, budget = sum([weights[i] for i in candidates]), surplus
        for i in candidates:
            addition = min(limit - holding[i], max(1, budget * weights[i] // pool), surplus)
            holding[i] = holding[i] + addition
            surplus = surplus - addition
    return np.array(holding)


def gaussian(stream_key, extent, spread, most, split=(), held_as=jnp.bfloat16):
    array = jax.random.normal(stream_key, extent, jnp.float32) * spread
    if len(split) > 0:
        array = levels(stream_key, extent, split, -0.22, 0.18) * array
    return jnp.clip(array, min=-most, max=most).astype(held_as)


def setup_inputs(seed: int = 0) -> dict:
    arg_keys = jax.random.split(jax.random.key(seed), 9)
    tokens = gaussian(arg_keys[0], (TOKENS, D), 1.0, 6.0, ((0, 128),))
    out_grad = gaussian(arg_keys[1], (TOKENS, D), 1.0, 6.0, ((0, 128),))
    route_ids_keys = jax.random.split(jax.random.fold_in(arg_keys[2], 1), TOKENS // TOK_DEV)
    route_ids_turns = jax.random.permutation(jax.random.fold_in(arg_keys[2], 3), TOKENS // TOK_DEV)
    route_ids = jax.vmap(lambda own, number: routed_block(jax.random.fold_in(arg_keys[2], 2), own, number, TOK_DEV, EXPERTS, TOP, CAP, 2))(route_ids_keys, route_ids_turns).reshape((TOKENS, TOP))
    route_logits = gaussian(arg_keys[3], (TOKENS, TOP), 2.0, 6.0, ((0, 128),), jnp.float32)
    gate_up = gaussian(arg_keys[4], (EXPERTS, 2, D, FFW), D ** -0.5, 0.09375, ((0, 32), (3, 4)))
    down = gaussian(arg_keys[5], (EXPERTS, FFW, D), FFW ** -0.5, 0.1875, ((0, 32), (1, 4)))
    moment1 = gaussian(arg_keys[6], (EXPERTS, FFW, D), 2.0, 8.0, ((0, 32), (1, 4)))
    moment2 = jnp.clip(jnp.exp(math.log(20.0) - 3.6888795 * jax.random.uniform(arg_keys[7], (EXPERTS, FFW, D), jnp.float32) ** levels(arg_keys[7], (EXPERTS, FFW, D), ((0, 32), (1, 4)), -0.2, 0.2)), 0.5, 20.0).astype(jnp.bfloat16)
    return {"tokens": tokens, "out_grad": out_grad, "route_ids": route_ids, "route_logits": route_logits, "gate_up": gate_up, "down": down, "moment1": moment1, "moment2": moment2}


ROUTE_SCALE = 2.5
BETA_ONE = 0.9
BETA_TWO = 0.95
LEARN_RATE = 0.001
DECAY = 0.1
EPSILON = 1e-08

def slot_tables(route_ids):
    devices_all = N_EXPERT * N_DP
    per_device = TOK_DEV * TOP
    blocks = route_ids.reshape(devices_all, per_device).astype(jnp.int32)
    onehot = (blocks[:, :, None] == jnp.arange(EXPERTS, dtype=jnp.int32)[None, None, :]).astype(jnp.int32)
    before = jnp.cumsum(onehot, axis=1) - onehot
    places = lax.optimization_barrier(jnp.sum(before * onehot, axis=2)).astype(jnp.int32)
    device_ids = jnp.broadcast_to(jnp.arange(devices_all, dtype=jnp.int32)[:, None], (devices_all, per_device))
    route_pos = jnp.broadcast_to(jnp.arange(per_device, dtype=jnp.int32)[None, :], (devices_all, per_device))
    token_row = device_ids * TOK_DEV + route_pos // TOP
    which_pick = route_pos % TOP
    flat_slot = ((blocks * N_DP + device_ids % N_DP) * N_EXPERT + device_ids // N_DP) * CAP + places
    flat_slot = flat_slot.reshape(-1).astype(jnp.int32)
    total_slots = EXPERTS * N_DP * N_EXPERT * CAP
    slot_token = jnp.zeros((total_slots,), jnp.int32).at[flat_slot].set(token_row.reshape(-1))
    slot_pick = jnp.zeros((total_slots,), jnp.int32).at[flat_slot].set(which_pick.reshape(-1))
    slot_live = jnp.zeros((total_slots,), jnp.float32).at[flat_slot].set(1.0)
    table_shape = (EXPERTS, N_DP * N_EXPERT * CAP)
    return (slot_token.reshape(table_shape), slot_pick.reshape(table_shape), slot_live.reshape(table_shape))

def reference(tokens, out_grad, route_ids, route_logits, gate_up, down, moment1, moment2):
    scores = jax.nn.sigmoid(route_logits.astype(jnp.float32))
    score_sum = lax.optimization_barrier(jnp.sum(scores, axis=1, keepdims=True))
    route_weight = (ROUTE_SCALE * scores / score_sum).astype(jnp.bfloat16)
    route_weight = lax.optimization_barrier(route_weight).astype(jnp.float32)
    slot_token, slot_pick, slot_live = slot_tables(route_ids)
    corr_one = 1.0 - BETA_ONE ** STEP
    corr_two = 1.0 - BETA_TWO ** STEP

    def per_expert(carry, inputs):
        grad_acc, affinity_acc = carry
        rows, pick_index, live, weights_gu, weights_down, first_old, second_old = inputs
        mask = live[:, None]
        xs_rows = jnp.take(tokens, rows, axis=0).astype(jnp.float32) * mask
        gs_rows = jnp.take(out_grad, rows, axis=0).astype(jnp.float32) * mask
        slot_weight = route_weight[rows, pick_index] * live
        gate_w = weights_gu[0].astype(jnp.float32)
        up_w = weights_gu[1].astype(jnp.float32)
        down_w = weights_down.astype(jnp.float32)
        pre_gate = jnp.dot(xs_rows, gate_w)
        pre_up = jnp.dot(xs_rows, up_w)
        sig_gate = jax.nn.sigmoid(pre_gate)
        silu_gate = pre_gate * sig_gate
        hidden = (silu_gate * pre_up).astype(jnp.bfloat16)
        hidden_wide = lax.optimization_barrier(hidden).astype(jnp.float32)
        back_raw = jnp.dot(gs_rows, down_w.T)
        affinity = lax.optimization_barrier(jnp.sum(hidden_wide * back_raw, axis=1)).astype(jnp.bfloat16)
        affinity = lax.optimization_barrier(affinity).astype(jnp.float32)
        scaled = (slot_weight[:, None] * gs_rows).astype(jnp.bfloat16)
        scaled = lax.optimization_barrier(scaled).astype(jnp.float32)
        parts = jnp.einsum('jsf,jsd->jfd', hidden_wide.reshape(N_DP, -1, FFW), scaled.reshape(N_DP, -1, D))
        parts = lax.optimization_barrier(parts.astype(jnp.bfloat16)).astype(jnp.float32)
        down_grad = lax.optimization_barrier(jnp.sum(parts, axis=0)) / N_DP
        back = slot_weight[:, None] * back_raw
        gate_grad = (back * pre_up * sig_gate * (1.0 + pre_gate * (1.0 - sig_gate))).astype(jnp.bfloat16)
        up_grad = (back * silu_gate).astype(jnp.bfloat16)
        gate_grad = lax.optimization_barrier(gate_grad).astype(jnp.float32)
        up_grad = lax.optimization_barrier(up_grad).astype(jnp.float32)
        route_in = (jnp.dot(gate_grad, gate_w.T) + jnp.dot(up_grad, up_w.T)).astype(jnp.bfloat16)
        route_in = lax.optimization_barrier(route_in).astype(jnp.float32)
        grad_acc = grad_acc.at[rows].add(route_in * mask)
        affinity_acc = affinity_acc.at[rows, pick_index].add(affinity * live)
        first = BETA_ONE * first_old.astype(jnp.float32) + (1.0 - BETA_ONE) * down_grad
        second = BETA_TWO * second_old.astype(jnp.float32) + (1.0 - BETA_TWO) * down_grad * down_grad
        update = first / corr_one / (jnp.sqrt(second / corr_two) + EPSILON) + DECAY * down_w
        new_weight = (down_w - LEARN_RATE * update).astype(jnp.bfloat16)
        return ((grad_acc, affinity_acc), (new_weight, first.astype(jnp.bfloat16), second.astype(jnp.bfloat16)))
    start = (jnp.zeros((TOKENS, D), jnp.float32), jnp.zeros((TOKENS, TOP), jnp.float32))
    (grad_acc, affinity_acc), (new_down, new_first, new_second) = lax.scan(per_expert, start, (slot_token, slot_pick, slot_live, gate_up, down, moment1, moment2))
    token_grad = grad_acc.astype(jnp.bfloat16)
    mixed = lax.optimization_barrier(jnp.sum(affinity_acc * scores, axis=1, keepdims=True)) / score_sum
    router_grad = ROUTE_SCALE * scores * (1.0 - scores) * (affinity_acc - mixed) / score_sum
    return (token_grad, router_grad, new_down, new_first, new_second)
```

```python
import jax
import jax.numpy as jnp
from jax import lax
from jax.sharding import PartitionSpec as P

STEP = 10


ROUTE_SCALE = 2.5
BETA_ONE = 0.9
BETA_TWO = 0.95
LEARN_RATE = 0.001
DECAY = 0.1
EPSILON = 1e-08
LANE = 128
HALVES = 2


def contract_last(left, right):
    return lax.dot_general(
        left, right, (((1,), (1,)), ((), ())), preferred_element_type=jnp.float32
    )


def contract_first(left, right):
    return lax.dot_general(
        left, right, (((0,), (0,)), ((), ())), preferred_element_type=jnp.float32
    )


def shards(tokens, out_grad, route_ids, route_logits, gate_up, down, moment1, moment2):
    experts = lax.axis_size("expert")
    data_ways = lax.axis_size("dp")
    tok_rows, model_width = tokens.shape
    top_count = route_ids.shape[1]
    local_ffw = down.shape[1]
    part_ffw = local_ffw // HALVES
    capacity = min(tok_rows, max(2, 5 * tok_rows * top_count // (4 * experts)))
    capacity = -(-capacity // 8) * 8
    slot_count = experts * capacity
    scores = jax.nn.sigmoid(route_logits)
    score_sum = jnp.sum(scores, axis=1, keepdims=True)
    route_weight = (ROUTE_SCALE * scores / score_sum).astype(jnp.bfloat16)
    flat_ids = route_ids.reshape(-1)
    onehot = (flat_ids[:, None] == jnp.arange(experts, dtype=jnp.int32)[None, :]).astype(jnp.int32)
    before = jnp.cumsum(onehot, axis=0) - onehot
    places = jnp.sum(before * onehot, axis=1)
    slot_index = flat_ids * capacity + places
    matched = (jnp.arange(slot_count, dtype=jnp.int32)[:, None] == slot_index[None, :]).astype(
        jnp.float32
    )
    tok_match = jnp.sum(matched.reshape(slot_count, tok_rows, top_count), axis=2).astype(
        jnp.bfloat16
    )
    send_weight = jnp.sum(matched * route_weight.astype(jnp.float32).reshape(-1)[None, :], axis=1)
    weight_block = jnp.zeros((slot_count, LANE), jnp.float32).at[:, 0].set(send_weight)
    payload = jnp.concatenate([tokens, out_grad], axis=1)
    send_rows = jnp.dot(tok_match, payload, preferred_element_type=jnp.float32)
    send_rows = jnp.concatenate([send_rows, weight_block], axis=1).astype(jnp.bfloat16)
    send_rows = send_rows.reshape(experts, capacity, 2 * model_width + LANE)

    full_down = lax.all_gather(down, "dp", axis=1, tiled=True)[0]
    gu_parts = [
        lax.all_gather(
            gate_up[:, :, :, h * part_ffw:(h + 1) * part_ffw], "dp", axis=3, tiled=True
        )[0]
        for h in range(HALVES)
    ]

    recv_rows = lax.all_to_all(send_rows, "expert", split_axis=0, concat_axis=0, tiled=True)
    recv_rows = recv_rows.reshape(slot_count, 2 * model_width + LANE)
    xs_rows = recv_rows[:, :model_width]
    gs_rows = recv_rows[:, model_width:2 * model_width]
    slot_weight = recv_rows[:, 2 * model_width].astype(jnp.float32)

    back_full = contract_last(gs_rows, full_down)
    back_full = back_full.reshape(slot_count, data_ways, HALVES, part_ffw)
    scaled = (slot_weight[:, None] * gs_rows.astype(jnp.float32)).astype(jnp.bfloat16)

    grad_parts = []
    affinity = jnp.zeros((slot_count,), jnp.float32)
    route_acc = jnp.zeros((slot_count, model_width), jnp.float32)
    for h in range(HALVES):
        gate_w = gu_parts[h][0]
        up_w = gu_parts[h][1]
        back_raw = back_full[:, :, h, :].reshape(slot_count, data_ways * part_ffw)
        pre_gate = jnp.dot(xs_rows, gate_w, preferred_element_type=jnp.float32)
        pre_up = jnp.dot(xs_rows, up_w, preferred_element_type=jnp.float32)
        sig_gate = jax.nn.sigmoid(pre_gate)
        silu_gate = pre_gate * sig_gate
        hidden = (silu_gate * pre_up).astype(jnp.bfloat16)
        affinity = affinity + jnp.sum(hidden.astype(jnp.float32) * back_raw, axis=1)
        local_grad = contract_first(hidden, scaled)
        grad_parts.append(
            lax.psum_scatter(local_grad.astype(jnp.bfloat16), "dp", scatter_dimension=0, tiled=True)
        )
        back = slot_weight[:, None] * back_raw
        gate_grad = (back * pre_up * sig_gate * (1.0 + pre_gate * (1.0 - sig_gate))).astype(
            jnp.bfloat16
        )
        up_grad = (back * silu_gate).astype(jnp.bfloat16)
        route_acc = route_acc + contract_last(gate_grad, gate_w) + contract_last(up_grad, up_w)

    affinity_block = jnp.zeros((slot_count, LANE), jnp.float32).at[:, 0].set(
        affinity.astype(jnp.bfloat16).astype(jnp.float32)
    )
    ret_rows = jnp.concatenate([route_acc.astype(jnp.bfloat16).astype(jnp.float32), affinity_block], axis=1)
    ret_rows = ret_rows.astype(jnp.bfloat16).reshape(experts, capacity, model_width + LANE)
    back_rows = lax.all_to_all(ret_rows, "expert", split_axis=0, concat_axis=0, tiled=True)
    back_rows = back_rows.reshape(slot_count, model_width + LANE)
    token_grad = contract_first(tok_match, back_rows[:, :model_width]).astype(jnp.bfloat16)
    back_affinity = back_rows[:, model_width].astype(jnp.float32)
    route_affinity = jnp.sum(matched * back_affinity[:, None], axis=0)
    route_affinity = route_affinity.reshape(tok_rows, top_count)
    mixed = jnp.sum(route_affinity * scores, axis=1, keepdims=True) / score_sum
    router_grad = ROUTE_SCALE * scores * (1.0 - scores) * (route_affinity - mixed) / score_sum

    grad_shard = jnp.concatenate(grad_parts, axis=0).astype(jnp.float32)
    down_grad = (grad_shard / data_ways)[None]
    corr_one = 1.0 - BETA_ONE**STEP
    corr_two = 1.0 - BETA_TWO**STEP
    down_wide = down.astype(jnp.float32)
    first = BETA_ONE * moment1.astype(jnp.float32) + (1.0 - BETA_ONE) * down_grad
    second = BETA_TWO * moment2.astype(jnp.float32) + (1.0 - BETA_TWO) * down_grad * down_grad
    update = first / corr_one / (jnp.sqrt(second / corr_two) + EPSILON) + DECAY * down_wide
    new_down = (down_wide - LEARN_RATE * update).astype(jnp.bfloat16)
    return (
        token_grad,
        router_grad,
        new_down,
        first.astype(jnp.bfloat16),
        second.astype(jnp.bfloat16),
    )


def solution(mesh):
    placed = (
        P(("expert", "dp"), None),
        P(("expert", "dp"), None),
        P(("expert", "dp"), None),
        P(("expert", "dp"), None),
        P("expert", None, None, "dp"),
        P("expert", "dp", None),
        P("expert", "dp", None),
        P("expert", "dp", None),
    )
    return jax.shard_map(
        shards,
        mesh=mesh,
        in_specs=placed,
        out_specs=(
            P(("expert", "dp"), None),
            P(("expert", "dp"), None),
            P("expert", "dp", None),
            P("expert", "dp", None),
            P("expert", "dp", None),
        ),
        check_vma=False,
    )
```

```python
import jax
import jax.numpy as jnp
from jax import lax
from jax.sharding import PartitionSpec as P

STEP = 10


ROUTE_SCALE = 2.5
BETA_ONE = 0.9
BETA_TWO = 0.95
LEARN_RATE = 0.001
DECAY = 0.1
EPSILON = 1e-08


def contract_last(left, right):
    return lax.dot_general(
        left, right, (((1,), (1,)), ((), ())), preferred_element_type=jnp.float32
    )


def contract_first(left, right):
    return lax.dot_general(
        left, right, (((0,), (0,)), ((), ())), preferred_element_type=jnp.float32
    )


def shards(tokens, out_grad, route_ids, route_logits, gate_up, down, moment1, moment2):
    experts = lax.axis_size("expert")
    data_ways = lax.axis_size("dp")
    tok_rows, model_width = tokens.shape
    top_count = route_ids.shape[1]
    capacity = min(tok_rows, max(2, 5 * tok_rows * top_count // (4 * experts)))
    side_row = capacity
    capacity = -(-(capacity + 1) // 8) * 8
    slot_count = experts * capacity
    scores = jax.nn.sigmoid(route_logits)
    score_sum = jnp.sum(scores, axis=1, keepdims=True)
    route_weight = (ROUTE_SCALE * scores / score_sum).astype(jnp.bfloat16)
    flat_ids = route_ids.reshape(-1)
    onehot = (flat_ids[:, None] == jnp.arange(experts, dtype=jnp.int32)[None, :]).astype(jnp.int32)
    before = jnp.cumsum(onehot, axis=0) - onehot
    places = jnp.sum(before * onehot, axis=1)
    slot_index = flat_ids * capacity + places
    matched = (jnp.arange(slot_count, dtype=jnp.int32)[:, None] == slot_index[None, :]).astype(
        jnp.float32
    )
    tok_match = jnp.sum(matched.reshape(slot_count, tok_rows, top_count), axis=2).astype(
        jnp.bfloat16
    )
    send_weight = jnp.sum(matched * route_weight.astype(jnp.float32).reshape(-1)[None, :], axis=1)
    payload = jnp.concatenate([tokens, out_grad], axis=1)
    send_rows = jnp.dot(tok_match, payload, preferred_element_type=jnp.float32).astype(jnp.bfloat16)
    send_rows = send_rows.reshape(experts, capacity, 2 * model_width)
    send_rows = send_rows.at[:, side_row, :capacity].set(
        send_weight.astype(jnp.bfloat16).reshape(experts, capacity)
    )

    full_gu = lax.all_gather(gate_up, "dp", axis=3, tiled=True)[0]
    full_down = lax.all_gather(down, "dp", axis=1, tiled=True)[0]

    recv_rows = lax.all_to_all(send_rows, "expert", split_axis=0, concat_axis=0, tiled=True)
    slot_weight = recv_rows[:, side_row, :capacity].reshape(slot_count).astype(jnp.float32)
    recv_rows = recv_rows.reshape(slot_count, 2 * model_width)
    xs_rows = recv_rows[:, :model_width]
    gs_rows = recv_rows[:, model_width:]

    gate_w = full_gu[0]
    up_w = full_gu[1]
    pre_gate = jnp.dot(xs_rows, gate_w, preferred_element_type=jnp.float32)
    pre_up = jnp.dot(xs_rows, up_w, preferred_element_type=jnp.float32)
    sig_gate = jax.nn.sigmoid(pre_gate)
    silu_gate = pre_gate * sig_gate
    hidden = (silu_gate * pre_up).astype(jnp.bfloat16)
    scaled = (slot_weight[:, None] * gs_rows.astype(jnp.float32)).astype(jnp.bfloat16)
    local_grad = contract_first(hidden, scaled)
    grad_shard = lax.psum_scatter(
        local_grad.astype(jnp.bfloat16), "dp", scatter_dimension=0, tiled=True
    ).astype(jnp.float32)
    back_raw = contract_last(gs_rows, full_down)
    affinity = jnp.sum(hidden.astype(jnp.float32) * back_raw, axis=1).astype(jnp.bfloat16)
    back = slot_weight[:, None] * back_raw
    gate_grad = (back * pre_up * sig_gate * (1.0 + pre_gate * (1.0 - sig_gate))).astype(
        jnp.bfloat16
    )
    up_grad = (back * silu_gate).astype(jnp.bfloat16)
    route_in = (contract_last(gate_grad, gate_w) + contract_last(up_grad, up_w)).astype(
        jnp.bfloat16
    )
    ret_rows = route_in.reshape(experts, capacity, model_width)
    ret_rows = ret_rows.at[:, side_row, :capacity].set(affinity.reshape(experts, capacity))
    back_rows = lax.all_to_all(ret_rows, "expert", split_axis=0, concat_axis=0, tiled=True)
    back_affinity = back_rows[:, side_row, :capacity].reshape(slot_count).astype(jnp.float32)
    back_rows = back_rows.reshape(slot_count, model_width)
    token_grad = contract_first(tok_match, back_rows).astype(jnp.bfloat16)
    route_affinity = jnp.sum(matched * back_affinity[:, None], axis=0)
    route_affinity = route_affinity.reshape(tok_rows, top_count)
    mixed = jnp.sum(route_affinity * scores, axis=1, keepdims=True) / score_sum
    router_grad = ROUTE_SCALE * scores * (1.0 - scores) * (route_affinity - mixed) / score_sum

    down_grad = (grad_shard / data_ways)[None]
    corr_one = 1.0 - BETA_ONE**STEP
    corr_two = 1.0 - BETA_TWO**STEP
    down_wide = down.astype(jnp.float32)
    first = BETA_ONE * moment1.astype(jnp.float32) + (1.0 - BETA_ONE) * down_grad
    second = BETA_TWO * moment2.astype(jnp.float32) + (1.0 - BETA_TWO) * down_grad * down_grad
    update = first / corr_one / (jnp.sqrt(second / corr_two) + EPSILON) + DECAY * down_wide
    new_down = (down_wide - LEARN_RATE * update).astype(jnp.bfloat16)
    return (
        token_grad,
        router_grad,
        new_down,
        first.astype(jnp.bfloat16),
        second.astype(jnp.bfloat16),
    )


def solution(mesh):
    placed = (
        P(("expert", "dp"), None),
        P(("expert", "dp"), None),
        P(("expert", "dp"), None),
        P(("expert", "dp"), None),
        P("expert", None, None, "dp"),
        P("expert", "dp", None),
        P("expert", "dp", None),
        P("expert", "dp", None),
    )
    return jax.shard_map(
        shards,
        mesh=mesh,
        in_specs=placed,
        out_specs=(
            P(("expert", "dp"), None),
            P(("expert", "dp"), None),
            P("expert", "dp", None),
            P("expert", "dp", None),
            P("expert", "dp", None),
        ),
        check_vma=False,
    )
```

```python
import jax
import jax.numpy as jnp
from jax import lax
from jax.sharding import PartitionSpec as P

STEP = 10


ROUTE_SCALE = 2.5
BETA_ONE = 0.9
BETA_TWO = 0.95
LEARN_RATE = 0.001
DECAY = 0.1
EPSILON = 1e-08


def contract_last(left, right):
    return lax.dot_general(
        left, right, (((1,), (1,)), ((), ())), preferred_element_type=jnp.float32
    )


def contract_first(left, right):
    return lax.dot_general(
        left, right, (((0,), (0,)), ((), ())), preferred_element_type=jnp.float32
    )


def shards(tokens, out_grad, route_ids, route_logits, gate_up, down, moment1, moment2):
    experts = lax.axis_size("expert")
    data_ways = lax.axis_size("dp")
    tok_rows, model_width = tokens.shape
    top_count = route_ids.shape[1]
    capacity = min(tok_rows, max(2, 5 * tok_rows * top_count // (4 * experts)))
    side_row = capacity
    capacity = -(-(capacity + 1) // 8) * 8
    slot_count = experts * capacity
    scores = jax.nn.sigmoid(route_logits)
    score_sum = jnp.sum(scores, axis=1, keepdims=True)
    route_weight = (ROUTE_SCALE * scores / score_sum).astype(jnp.bfloat16)
    flat_ids = route_ids.reshape(-1)
    onehot = (flat_ids[:, None] == jnp.arange(experts, dtype=jnp.int32)[None, :]).astype(jnp.int32)
    before = jnp.cumsum(onehot, axis=0) - onehot
    places = jnp.sum(before * onehot, axis=1)
    slot_index = flat_ids * capacity + places
    matched = (jnp.arange(slot_count, dtype=jnp.int32)[:, None] == slot_index[None, :]).astype(
        jnp.float32
    )
    tok_match = jnp.sum(matched.reshape(slot_count, tok_rows, top_count), axis=2).astype(
        jnp.bfloat16
    )
    send_weight = jnp.sum(matched * route_weight.astype(jnp.float32).reshape(-1)[None, :], axis=1)
    payload = jnp.concatenate([tokens, out_grad], axis=1)
    send_rows = jnp.dot(tok_match, payload, preferred_element_type=jnp.float32).astype(jnp.bfloat16)
    send_rows = send_rows.reshape(experts, capacity, 2 * model_width)
    send_rows = send_rows.at[:, side_row, :capacity].set(
        send_weight.astype(jnp.bfloat16).reshape(experts, capacity)
    )

    full_gu = lax.all_gather(gate_up, "dp", axis=3, tiled=True)[0]
    full_down = lax.all_gather(down, "dp", axis=1, tiled=True)[0]

    recv_rows = lax.all_to_all(send_rows, "expert", split_axis=0, concat_axis=0, tiled=True)
    slot_weight = recv_rows[:, side_row, :capacity].reshape(slot_count).astype(jnp.float32)
    recv_rows = recv_rows.reshape(slot_count, 2 * model_width)
    xs_rows = recv_rows[:, :model_width]
    gs_rows = recv_rows[:, model_width:]

    gate_w = full_gu[0]
    up_w = full_gu[1]
    pre_gate = jnp.dot(xs_rows, gate_w, preferred_element_type=jnp.float32)
    pre_up = jnp.dot(xs_rows, up_w, preferred_element_type=jnp.float32)
    sig_gate = jax.nn.sigmoid(pre_gate)
    silu_gate = pre_gate * sig_gate
    hidden = (silu_gate * pre_up).astype(jnp.bfloat16)
    scaled = (slot_weight[:, None] * gs_rows.astype(jnp.float32)).astype(jnp.bfloat16)
    local_grad = contract_first(hidden, scaled).astype(jnp.bfloat16)
    local_grad, gs_rows = lax.optimization_barrier((local_grad, gs_rows))
    grad_shard = lax.psum_scatter(local_grad, "dp", scatter_dimension=0, tiled=True).astype(
        jnp.float32
    )
    back_raw = contract_last(gs_rows, full_down)
    affinity = jnp.sum(hidden.astype(jnp.float32) * back_raw, axis=1).astype(jnp.bfloat16)
    back = slot_weight[:, None] * back_raw
    gate_grad = (back * pre_up * sig_gate * (1.0 + pre_gate * (1.0 - sig_gate))).astype(
        jnp.bfloat16
    )
    up_grad = (back * silu_gate).astype(jnp.bfloat16)
    half_width = model_width // 2
    pieces = []
    for c in range(2):
        cols = slice(c * half_width, (c + 1) * half_width)
        route_in = (
            contract_last(gate_grad, gate_w[cols]) + contract_last(up_grad, up_w[cols])
        ).astype(jnp.bfloat16)
        ret_rows = route_in.reshape(experts, capacity, half_width)
        if c == 0:
            ret_rows = ret_rows.at[:, side_row, :capacity].set(affinity.reshape(experts, capacity))
        pieces.append(lax.all_to_all(ret_rows, "expert", split_axis=0, concat_axis=0, tiled=True))
    back_affinity = pieces[0][:, side_row, :capacity].reshape(slot_count).astype(jnp.float32)
    token_grad = jnp.concatenate(
        [contract_first(tok_match, p.reshape(slot_count, half_width)) for p in pieces], axis=1
    ).astype(jnp.bfloat16)
    route_affinity = jnp.sum(matched * back_affinity[:, None], axis=0)
    route_affinity = route_affinity.reshape(tok_rows, top_count)
    mixed = jnp.sum(route_affinity * scores, axis=1, keepdims=True) / score_sum
    router_grad = ROUTE_SCALE * scores * (1.0 - scores) * (route_affinity - mixed) / score_sum

    down_grad = (grad_shard / data_ways)[None]
    corr_one = 1.0 - BETA_ONE**STEP
    corr_two = 1.0 - BETA_TWO**STEP
    down_wide = down.astype(jnp.float32)
    first = BETA_ONE * moment1.astype(jnp.float32) + (1.0 - BETA_ONE) * down_grad
    second = BETA_TWO * moment2.astype(jnp.float32) + (1.0 - BETA_TWO) * down_grad * down_grad
    update = first / corr_one / (jnp.sqrt(second / corr_two) + EPSILON) + DECAY * down_wide
    new_down = (down_wide - LEARN_RATE * update).astype(jnp.bfloat16)
    return (
        token_grad,
        router_grad,
        new_down,
        first.astype(jnp.bfloat16),
        second.astype(jnp.bfloat16),
    )


def solution(mesh):
    placed = (
        P(("expert", "dp"), None),
        P(("expert", "dp"), None),
        P(("expert", "dp"), None),
        P(("expert", "dp"), None),
        P("expert", None, None, "dp"),
        P("expert", "dp", None),
        P("expert", "dp", None),
        P("expert", "dp", None),
    )
    return jax.shard_map(
        shards,
        mesh=mesh,
        in_specs=placed,
        out_specs=(
            P(("expert", "dp"), None),
            P(("expert", "dp"), None),
            P("expert", "dp", None),
            P("expert", "dp", None),
            P("expert", "dp", None),
        ),
        check_vma=False,
    )
```

```python
import jax
import jax.numpy as jnp
from jax import lax
from jax.sharding import PartitionSpec as P

STEP = 10


ROUTE_SCALE = 2.5
BETA_ONE = 0.9
BETA_TWO = 0.95
LEARN_RATE = 0.001
DECAY = 0.1
EPSILON = 1e-08


def contract_last(left, right):
    return lax.dot_general(
        left, right, (((1,), (1,)), ((), ())), preferred_element_type=jnp.float32
    )


def contract_first(left, right):
    return lax.dot_general(
        left, right, (((0,), (0,)), ((), ())), preferred_element_type=jnp.float32
    )


def shards(tokens, out_grad, route_ids, route_logits, gate_up, down, moment1, moment2):
    experts = lax.axis_size("expert")
    data_ways = lax.axis_size("dp")
    tok_rows, model_width = tokens.shape
    top_count = route_ids.shape[1]
    capacity = min(tok_rows, max(2, 5 * tok_rows * top_count // (4 * experts)))
    side_row = capacity
    capacity = -(-(capacity + 1) // 8) * 8
    slot_count = experts * capacity
    scores = jax.nn.sigmoid(route_logits)
    score_sum = jnp.sum(scores, axis=1, keepdims=True)
    route_weight = (ROUTE_SCALE * scores / score_sum).astype(jnp.bfloat16)
    flat_ids = route_ids.reshape(-1)
    onehot = (flat_ids[:, None] == jnp.arange(experts, dtype=jnp.int32)[None, :]).astype(jnp.int32)
    before = jnp.cumsum(onehot, axis=0) - onehot
    places = jnp.sum(before * onehot, axis=1)
    slot_index = flat_ids * capacity + places
    matched = (jnp.arange(slot_count, dtype=jnp.int32)[:, None] == slot_index[None, :]).astype(
        jnp.float32
    )
    tok_match = jnp.sum(matched.reshape(slot_count, tok_rows, top_count), axis=2).astype(
        jnp.bfloat16
    )
    send_weight = jnp.sum(matched * route_weight.astype(jnp.float32).reshape(-1)[None, :], axis=1)
    payload = jnp.concatenate([tokens, out_grad], axis=1)
    send_rows = jnp.dot(tok_match, payload, preferred_element_type=jnp.float32).astype(jnp.bfloat16)
    send_rows = send_rows.reshape(experts, capacity, 2 * model_width)
    send_rows = send_rows.at[:, side_row, :capacity].set(
        send_weight.astype(jnp.bfloat16).reshape(experts, capacity)
    )

    full_gu = lax.all_gather(gate_up, "dp", axis=3, tiled=True)[0]
    local_ffw = down.shape[1]
    part_ffw = local_ffw // 2
    down_parts = [
        lax.all_gather(down[:, h * part_ffw:(h + 1) * part_ffw], "dp", axis=1, tiled=True)[0]
        for h in range(2)
    ]

    recv_rows = lax.all_to_all(send_rows, "expert", split_axis=0, concat_axis=0, tiled=True)
    slot_weight = recv_rows[:, side_row, :capacity].reshape(slot_count).astype(jnp.float32)
    recv_rows = recv_rows.reshape(slot_count, 2 * model_width)
    xs_rows = recv_rows[:, :model_width]
    gs_rows = recv_rows[:, model_width:]
    scaled = (slot_weight[:, None] * gs_rows.astype(jnp.float32)).astype(jnp.bfloat16)

    def half_cols(w, h):
        return w.reshape(model_width, data_ways, 2, part_ffw)[:, :, h, :].reshape(
            model_width, data_ways * part_ffw
        )

    gate_h, up_h, pre_gate_h, pre_up_h, sig_h, silu_h, hidden_h, grad_h = ([] for _ in range(8))
    for h in range(2):
        gate_w = half_cols(full_gu[0], h)
        up_w = half_cols(full_gu[1], h)
        pre_gate = jnp.dot(xs_rows, gate_w, preferred_element_type=jnp.float32)
        pre_up = jnp.dot(xs_rows, up_w, preferred_element_type=jnp.float32)
        sig_gate = jax.nn.sigmoid(pre_gate)
        silu_gate = pre_gate * sig_gate
        hidden = (silu_gate * pre_up).astype(jnp.bfloat16)
        local_grad = contract_first(hidden, scaled).astype(jnp.bfloat16)
        for lst, val in zip(
            (gate_h, up_h, pre_gate_h, pre_up_h, sig_h, silu_h, hidden_h, grad_h),
            (gate_w, up_w, pre_gate, pre_up, sig_gate, silu_gate, hidden, local_grad),
        ):
            lst.append(val)
    local_grad = jnp.stack(
        [g.reshape(data_ways, part_ffw, model_width) for g in grad_h], axis=1
    ).reshape(data_ways * local_ffw, model_width)
    local_grad, gs_rows = lax.optimization_barrier((local_grad, gs_rows))
    grad_shard = lax.psum_scatter(local_grad, "dp", scatter_dimension=0, tiled=True).astype(
        jnp.float32
    )
    half_width = model_width // 2
    affinity = jnp.zeros((slot_count,), jnp.float32)
    route_acc = [jnp.zeros((slot_count, half_width), jnp.float32) for _ in range(2)]
    for h in range(2):
        back_raw = contract_last(gs_rows, down_parts[h])
        affinity = affinity + jnp.sum(hidden_h[h].astype(jnp.float32) * back_raw, axis=1)
        back = slot_weight[:, None] * back_raw
        pre_gate, pre_up, sig_gate, silu_gate = pre_gate_h[h], pre_up_h[h], sig_h[h], silu_h[h]
        gate_grad = (back * pre_up * sig_gate * (1.0 + pre_gate * (1.0 - sig_gate))).astype(
            jnp.bfloat16
        )
        up_grad = (back * silu_gate).astype(jnp.bfloat16)
        for c in range(2):
            cols = slice(c * half_width, (c + 1) * half_width)
            route_acc[c] = (
                route_acc[c]
                + contract_last(gate_grad, gate_h[h][cols])
                + contract_last(up_grad, up_h[h][cols])
            )
        if h == 0:
            *route_acc, gs_rows = lax.optimization_barrier((*route_acc, gs_rows))
    affinity = affinity.astype(jnp.bfloat16)
    pieces = []
    for c in range(2):
        ret_rows = route_acc[c].astype(jnp.bfloat16).reshape(experts, capacity, half_width)
        if c == 0:
            ret_rows = ret_rows.at[:, side_row, :capacity].set(affinity.reshape(experts, capacity))
        pieces.append(lax.all_to_all(ret_rows, "expert", split_axis=0, concat_axis=0, tiled=True))
    back_affinity = pieces[0][:, side_row, :capacity].reshape(slot_count).astype(jnp.float32)
    token_grad = jnp.concatenate(
        [contract_first(tok_match, p.reshape(slot_count, half_width)) for p in pieces], axis=1
    ).astype(jnp.bfloat16)
    route_affinity = jnp.sum(matched * back_affinity[:, None], axis=0)
    route_affinity = route_affinity.reshape(tok_rows, top_count)
    mixed = jnp.sum(route_affinity * scores, axis=1, keepdims=True) / score_sum
    router_grad = ROUTE_SCALE * scores * (1.0 - scores) * (route_affinity - mixed) / score_sum

    down_grad = (grad_shard / data_ways)[None]
    corr_one = 1.0 - BETA_ONE**STEP
    corr_two = 1.0 - BETA_TWO**STEP
    down_wide = down.astype(jnp.float32)
    first = BETA_ONE * moment1.astype(jnp.float32) + (1.0 - BETA_ONE) * down_grad
    second = BETA_TWO * moment2.astype(jnp.float32) + (1.0 - BETA_TWO) * down_grad * down_grad
    update = first / corr_one / (jnp.sqrt(second / corr_two) + EPSILON) + DECAY * down_wide
    new_down = (down_wide - LEARN_RATE * update).astype(jnp.bfloat16)
    return (
        token_grad,
        router_grad,
        new_down,
        first.astype(jnp.bfloat16),
        second.astype(jnp.bfloat16),
    )


def solution(mesh):
    placed = (
        P(("expert", "dp"), None),
        P(("expert", "dp"), None),
        P(("expert", "dp"), None),
        P(("expert", "dp"), None),
        P("expert", None, None, "dp"),
        P("expert", "dp", None),
        P("expert", "dp", None),
        P("expert", "dp", None),
    )
    return jax.shard_map(
        shards,
        mesh=mesh,
        in_specs=placed,
        out_specs=(
            P(("expert", "dp"), None),
            P(("expert", "dp"), None),
            P("expert", "dp", None),
            P("expert", "dp", None),
            P("expert", "dp", None),
        ),
        check_vma=False,
    )
```

```python
import jax
import jax.numpy as jnp
from jax import lax
from jax.sharding import PartitionSpec as P

STEP = 10


ROUTE_SCALE = 2.5
BETA_ONE = 0.9
BETA_TWO = 0.95
LEARN_RATE = 0.001
DECAY = 0.1
EPSILON = 1e-08


def contract_last(left, right):
    return lax.dot_general(
        left, right, (((1,), (1,)), ((), ())), preferred_element_type=jnp.float32
    )


def contract_first(left, right):
    return lax.dot_general(
        left, right, (((0,), (0,)), ((), ())), preferred_element_type=jnp.float32
    )


def shards(tokens, out_grad, route_ids, route_logits, gate_up, down, moment1, moment2):
    experts = lax.axis_size("expert")
    data_ways = lax.axis_size("dp")
    tok_rows, model_width = tokens.shape
    top_count = route_ids.shape[1]
    capacity = min(tok_rows, max(2, 5 * tok_rows * top_count // (4 * experts)))
    side_row = capacity
    capacity = -(-(capacity + 1) // 8) * 8
    slot_count = experts * capacity
    scores = jax.nn.sigmoid(route_logits)
    score_sum = jnp.sum(scores, axis=1, keepdims=True)
    route_weight = (ROUTE_SCALE * scores / score_sum).astype(jnp.bfloat16)
    flat_ids = route_ids.reshape(-1)
    onehot = (flat_ids[:, None] == jnp.arange(experts, dtype=jnp.int32)[None, :]).astype(jnp.int32)
    before = jnp.cumsum(onehot, axis=0) - onehot
    places = jnp.sum(before * onehot, axis=1)
    slot_index = flat_ids * capacity + places
    matched = (jnp.arange(slot_count, dtype=jnp.int32)[:, None] == slot_index[None, :]).astype(
        jnp.float32
    )
    tok_match = jnp.sum(matched.reshape(slot_count, tok_rows, top_count), axis=2).astype(
        jnp.bfloat16
    )
    send_weight = jnp.sum(matched * route_weight.astype(jnp.float32).reshape(-1)[None, :], axis=1)
    payload = jnp.concatenate([tokens, out_grad], axis=1)
    send_rows = jnp.dot(tok_match, payload, preferred_element_type=jnp.float32).astype(jnp.bfloat16)
    send_rows = send_rows.reshape(experts, capacity, 2 * model_width)
    send_rows = send_rows.at[:, side_row, :capacity].set(
        send_weight.astype(jnp.bfloat16).reshape(experts, capacity)
    )

    full_gu = lax.all_gather(gate_up, "dp", axis=3, tiled=True)[0]
    full_down = lax.all_gather(down, "dp", axis=1, tiled=True)[0]

    recv_rows = lax.all_to_all(send_rows, "expert", split_axis=0, concat_axis=0, tiled=True)
    slot_weight = recv_rows[:, side_row, :capacity].reshape(slot_count).astype(jnp.float32)
    recv_rows = recv_rows.reshape(slot_count, 2 * model_width)
    xs_rows = recv_rows[:, :model_width]
    gs_rows = recv_rows[:, model_width:]

    gate_w = full_gu[0]
    up_w = full_gu[1]
    pre_gate = jnp.dot(xs_rows, gate_w, preferred_element_type=jnp.float32)
    pre_up = jnp.dot(xs_rows, up_w, preferred_element_type=jnp.float32)
    sig_gate = jax.nn.sigmoid(pre_gate)
    silu_gate = pre_gate * sig_gate
    hidden = (silu_gate * pre_up).astype(jnp.bfloat16)
    scaled = (slot_weight[:, None] * gs_rows.astype(jnp.float32)).astype(jnp.bfloat16)
    local_grad = contract_first(hidden, scaled).astype(jnp.bfloat16)
    local_grad, gs_rows = lax.optimization_barrier((local_grad, gs_rows))
    grad_shard = lax.psum_scatter(local_grad, "dp", scatter_dimension=0, tiled=True).astype(
        jnp.float32
    )
    back_raw = contract_last(gs_rows, full_down)
    affinity = jnp.sum(hidden.astype(jnp.float32) * back_raw, axis=1).astype(jnp.bfloat16)
    back = slot_weight[:, None] * back_raw
    gate_grad = (back * pre_up * sig_gate * (1.0 + pre_gate * (1.0 - sig_gate))).astype(
        jnp.bfloat16
    )
    up_grad = (back * silu_gate).astype(jnp.bfloat16)
    grads = jnp.stack([gate_grad, up_grad], axis=1)
    half_width = model_width // 2
    pieces = []
    for c in range(2):
        cols = slice(c * half_width, (c + 1) * half_width)
        route_in = lax.dot_general(
            grads, full_gu[:, cols], (((1, 2), (0, 2)), ((), ())),
            preferred_element_type=jnp.float32,
        ).astype(jnp.bfloat16)
        ret_rows = route_in.reshape(experts, capacity, half_width)
        if c == 0:
            ret_rows = ret_rows.at[:, side_row, :capacity].set(affinity.reshape(experts, capacity))
        pieces.append(lax.all_to_all(ret_rows, "expert", split_axis=0, concat_axis=0, tiled=True))
    back_affinity = pieces[0][:, side_row, :capacity].reshape(slot_count).astype(jnp.float32)
    token_grad = jnp.concatenate(
        [contract_first(tok_match, p.reshape(slot_count, half_width)) for p in pieces], axis=1
    ).astype(jnp.bfloat16)
    route_affinity = jnp.sum(matched * back_affinity[:, None], axis=0)
    route_affinity = route_affinity.reshape(tok_rows, top_count)
    mixed = jnp.sum(route_affinity * scores, axis=1, keepdims=True) / score_sum
    router_grad = ROUTE_SCALE * scores * (1.0 - scores) * (route_affinity - mixed) / score_sum

    down_grad = (grad_shard / data_ways)[None]
    corr_one = 1.0 - BETA_ONE**STEP
    corr_two = 1.0 - BETA_TWO**STEP
    down_wide = down.astype(jnp.float32)
    first = BETA_ONE * moment1.astype(jnp.float32) + (1.0 - BETA_ONE) * down_grad
    second = BETA_TWO * moment2.astype(jnp.float32) + (1.0 - BETA_TWO) * down_grad * down_grad
    update = first / corr_one / (jnp.sqrt(second / corr_two) + EPSILON) + DECAY * down_wide
    new_down = (down_wide - LEARN_RATE * update).astype(jnp.bfloat16)
    return (
        token_grad,
        router_grad,
        new_down,
        first.astype(jnp.bfloat16),
        second.astype(jnp.bfloat16),
    )


def solution(mesh):
    placed = (
        P(("expert", "dp"), None),
        P(("expert", "dp"), None),
        P(("expert", "dp"), None),
        P(("expert", "dp"), None),
        P("expert", None, None, "dp"),
        P("expert", "dp", None),
        P("expert", "dp", None),
        P("expert", "dp", None),
    )
    return jax.shard_map(
        shards,
        mesh=mesh,
        in_specs=placed,
        out_specs=(
            P(("expert", "dp"), None),
            P(("expert", "dp"), None),
            P("expert", "dp", None),
            P("expert", "dp", None),
            P("expert", "dp", None),
        ),
        check_vma=False,
    )
```

```python
import jax
import jax.numpy as jnp
from jax import lax
from jax.sharding import PartitionSpec as P

STEP = 10


ROUTE_SCALE = 2.5
BETA_ONE = 0.9
BETA_TWO = 0.95
LEARN_RATE = 0.001
DECAY = 0.1
EPSILON = 1e-08


def contract_last(left, right):
    return lax.dot_general(
        left, right, (((1,), (1,)), ((), ())), preferred_element_type=jnp.float32
    )


def contract_first(left, right):
    return lax.dot_general(
        left, right, (((0,), (0,)), ((), ())), preferred_element_type=jnp.float32
    )


def shards(tokens, out_grad, route_ids, route_logits, gate_up, down, moment1, moment2):
    experts = lax.axis_size("expert")
    data_ways = lax.axis_size("dp")
    tok_rows, model_width = tokens.shape
    top_count = route_ids.shape[1]
    capacity = min(tok_rows, max(2, 5 * tok_rows * top_count // (4 * experts)))
    side_row = capacity
    capacity = -(-(capacity + 1) // 8) * 8
    slot_count = experts * capacity
    scores = jax.nn.sigmoid(route_logits)
    score_sum = jnp.sum(scores, axis=1, keepdims=True)
    route_weight = (ROUTE_SCALE * scores / score_sum).astype(jnp.bfloat16)
    flat_ids = route_ids.reshape(-1)
    onehot = (flat_ids[:, None] == jnp.arange(experts, dtype=jnp.int32)[None, :]).astype(jnp.int32)
    before = jnp.cumsum(onehot, axis=0) - onehot
    places = jnp.sum(before * onehot, axis=1)
    slot_index = flat_ids * capacity + places
    matched = (jnp.arange(slot_count, dtype=jnp.int32)[:, None] == slot_index[None, :]).astype(
        jnp.float32
    )
    tok_match = jnp.sum(matched.reshape(slot_count, tok_rows, top_count), axis=2).astype(
        jnp.bfloat16
    )
    send_weight = jnp.sum(matched * route_weight.astype(jnp.float32).reshape(-1)[None, :], axis=1)
    payload = jnp.concatenate([tokens, out_grad], axis=1)
    send_rows = jnp.dot(tok_match, payload, preferred_element_type=jnp.float32).astype(jnp.bfloat16)
    send_rows = send_rows.reshape(experts, capacity, 2 * model_width)
    send_rows = send_rows.at[:, side_row, :capacity].set(
        send_weight.astype(jnp.bfloat16).reshape(experts, capacity)
    )

    full_gu = lax.all_gather(gate_up, "dp", axis=3, tiled=True)[0]
    full_down = lax.all_gather(down, "dp", axis=1, tiled=True)[0]

    recv_rows = lax.all_to_all(send_rows, "expert", split_axis=0, concat_axis=0, tiled=True)
    slot_weight = recv_rows[:, side_row, :capacity].reshape(slot_count).astype(jnp.float32)
    recv_rows = recv_rows.reshape(slot_count, 2 * model_width)
    xs_rows = recv_rows[:, :model_width]
    gs_rows = recv_rows[:, model_width:]

    gate_w = full_gu[0]
    up_w = full_gu[1]
    pre_gate = jnp.dot(xs_rows, gate_w, preferred_element_type=jnp.float32)
    pre_up = jnp.dot(xs_rows, up_w, preferred_element_type=jnp.float32)
    sig_gate = jax.nn.sigmoid(pre_gate)
    silu_gate = pre_gate * sig_gate
    hidden = (silu_gate * pre_up).astype(jnp.bfloat16)
    scaled = (slot_weight[:, None] * gs_rows.astype(jnp.float32)).astype(jnp.bfloat16)
    local_grad = contract_first(hidden, scaled).astype(jnp.bfloat16)
    local_grad, gs_rows = lax.optimization_barrier((local_grad, gs_rows))
    grad_shard = lax.psum_scatter(local_grad, "dp", scatter_dimension=0, tiled=True).astype(
        jnp.float32
    )
    back_raw = contract_last(gs_rows, full_down)
    affinity = jnp.sum(hidden.astype(jnp.float32) * back_raw, axis=1).astype(jnp.bfloat16)
    back = slot_weight[:, None] * back_raw
    gate_grad = (back * pre_up * sig_gate * (1.0 + pre_gate * (1.0 - sig_gate))).astype(
        jnp.bfloat16
    )
    up_grad = (back * silu_gate).astype(jnp.bfloat16)
    grads = jnp.stack([gate_grad, up_grad], axis=1)
    route_in = lax.dot_general(
        grads, full_gu, (((1, 2), (0, 2)), ((), ())), preferred_element_type=jnp.float32
    ).astype(jnp.bfloat16)
    ret_rows = route_in.reshape(experts, capacity, model_width)
    ret_rows = ret_rows.at[:, side_row, :capacity].set(affinity.reshape(experts, capacity))
    back_rows = lax.all_to_all(ret_rows, "expert", split_axis=0, concat_axis=0, tiled=True)
    back_affinity = back_rows[:, side_row, :capacity].reshape(slot_count).astype(jnp.float32)
    token_grad = contract_first(tok_match, back_rows.reshape(slot_count, model_width)).astype(
        jnp.bfloat16
    )
    route_affinity = jnp.sum(matched * back_affinity[:, None], axis=0)
    route_affinity = route_affinity.reshape(tok_rows, top_count)
    mixed = jnp.sum(route_affinity * scores, axis=1, keepdims=True) / score_sum
    router_grad = ROUTE_SCALE * scores * (1.0 - scores) * (route_affinity - mixed) / score_sum

    down_grad = (grad_shard / data_ways)[None]
    corr_one = 1.0 - BETA_ONE**STEP
    corr_two = 1.0 - BETA_TWO**STEP
    down_wide = down.astype(jnp.float32)
    first = BETA_ONE * moment1.astype(jnp.float32) + (1.0 - BETA_ONE) * down_grad
    second = BETA_TWO * moment2.astype(jnp.float32) + (1.0 - BETA_TWO) * down_grad * down_grad
    update = first / corr_one / (jnp.sqrt(second / corr_two) + EPSILON) + DECAY * down_wide
    new_down = (down_wide - LEARN_RATE * update).astype(jnp.bfloat16)
    return (
        token_grad,
        router_grad,
        new_down,
        first.astype(jnp.bfloat16),
        second.astype(jnp.bfloat16),
    )


def solution(mesh):
    placed = (
        P(("expert", "dp"), None),
        P(("expert", "dp"), None),
        P(("expert", "dp"), None),
        P(("expert", "dp"), None),
        P("expert", None, None, "dp"),
        P("expert", "dp", None),
        P("expert", "dp", None),
        P("expert", "dp", None),
    )
    return jax.shard_map(
        shards,
        mesh=mesh,
        in_specs=placed,
        out_specs=(
            P(("expert", "dp"), None),
            P(("expert", "dp"), None),
            P("expert", "dp", None),
            P("expert", "dp", None),
            P("expert", "dp", None),
        ),
        check_vma=False,
    )
```

```python
import jax
import jax.numpy as jnp
from jax import lax
from jax.sharding import PartitionSpec as P

STEP = 10


ROUTE_SCALE = 2.5
BETA_ONE = 0.9
BETA_TWO = 0.95
LEARN_RATE = 0.001
DECAY = 0.1
EPSILON = 1e-08


def contract_last(left, right):
    return lax.dot_general(
        left, right, (((1,), (1,)), ((), ())), preferred_element_type=jnp.float32
    )


def contract_first(left, right):
    return lax.dot_general(
        left, right, (((0,), (0,)), ((), ())), preferred_element_type=jnp.float32
    )


def shards(tokens, out_grad, route_ids, route_logits, gate_up, down, moment1, moment2):
    experts = lax.axis_size("expert")
    data_ways = lax.axis_size("dp")
    tok_rows, model_width = tokens.shape
    top_count = route_ids.shape[1]
    capacity = min(tok_rows, max(2, 5 * tok_rows * top_count // (4 * experts)))
    side_row = capacity
    capacity = -(-(capacity + 1) // 8) * 8
    slot_count = experts * capacity
    scores = jax.nn.sigmoid(route_logits)
    score_sum = jnp.sum(scores, axis=1, keepdims=True)
    route_weight = (ROUTE_SCALE * scores / score_sum).astype(jnp.bfloat16)
    flat_ids = route_ids.reshape(-1)
    onehot = (flat_ids[:, None] == jnp.arange(experts, dtype=jnp.int32)[None, :]).astype(jnp.int32)
    before = jnp.cumsum(onehot, axis=0) - onehot
    places = jnp.sum(before * onehot, axis=1)
    slot_index = flat_ids * capacity + places
    matched = (jnp.arange(slot_count, dtype=jnp.int32)[:, None] == slot_index[None, :]).astype(
        jnp.float32
    )
    tok_match = jnp.sum(matched.reshape(slot_count, tok_rows, top_count), axis=2).astype(
        jnp.bfloat16
    )
    send_weight = jnp.sum(matched * route_weight.astype(jnp.float32).reshape(-1)[None, :], axis=1)
    payload = jnp.concatenate([tokens, out_grad], axis=1)
    send_rows = jnp.dot(tok_match, payload, preferred_element_type=jnp.float32).astype(jnp.bfloat16)
    send_rows = send_rows.reshape(experts, capacity, 2 * model_width)
    send_rows = send_rows.at[:, side_row, :capacity].set(
        send_weight.astype(jnp.bfloat16).reshape(experts, capacity)
    )

    full_gu = lax.all_gather(gate_up, "dp", axis=3, tiled=True)[0]
    full_down = lax.all_gather(down, "dp", axis=1, tiled=True)[0]

    recv_rows = lax.all_to_all(send_rows, "expert", split_axis=0, concat_axis=0, tiled=True)
    slot_weight = recv_rows[:, side_row, :capacity].reshape(slot_count).astype(jnp.float32)
    recv_rows = recv_rows.reshape(slot_count, 2 * model_width)
    xs_rows = recv_rows[:, :model_width]
    gs_rows = recv_rows[:, model_width:]

    gate_w = full_gu[0]
    up_w = full_gu[1]
    pre_gate = jnp.dot(xs_rows, gate_w, preferred_element_type=jnp.float32)
    pre_up = jnp.dot(xs_rows, up_w, preferred_element_type=jnp.float32)
    sig_gate = jax.nn.sigmoid(pre_gate)
    silu_gate = pre_gate * sig_gate
    hidden = (silu_gate * pre_up).astype(jnp.bfloat16)
    scaled = (slot_weight[:, None] * gs_rows.astype(jnp.float32)).astype(jnp.bfloat16)
    local_grad = contract_first(hidden, scaled).astype(jnp.bfloat16)
    gate_factor = slot_weight[:, None] * (pre_up * sig_gate * (1.0 + pre_gate * (1.0 - sig_gate)))
    up_factor = slot_weight[:, None] * silu_gate
    factors = jnp.stack([gate_factor, up_factor], axis=1)
    local_grad, factors, gs_rows = lax.optimization_barrier((local_grad, factors, gs_rows))
    grad_shard = lax.psum_scatter(local_grad, "dp", scatter_dimension=0, tiled=True).astype(
        jnp.float32
    )
    back_raw = contract_last(gs_rows, full_down)
    affinity = jnp.sum(hidden.astype(jnp.float32) * back_raw, axis=1).astype(jnp.bfloat16)
    grads = (back_raw[:, None, :] * factors).astype(jnp.bfloat16)
    route_in = lax.dot_general(
        grads, full_gu, (((1, 2), (0, 2)), ((), ())), preferred_element_type=jnp.float32
    ).astype(jnp.bfloat16)
    ret_rows = route_in.reshape(experts, capacity, model_width)
    ret_rows = ret_rows.at[:, side_row, :capacity].set(affinity.reshape(experts, capacity))
    back_rows = lax.all_to_all(ret_rows, "expert", split_axis=0, concat_axis=0, tiled=True)
    back_affinity = back_rows[:, side_row, :capacity].reshape(slot_count).astype(jnp.float32)
    token_grad = contract_first(tok_match, back_rows.reshape(slot_count, model_width)).astype(
        jnp.bfloat16
    )
    route_affinity = jnp.sum(matched * back_affinity[:, None], axis=0)
    route_affinity = route_affinity.reshape(tok_rows, top_count)
    mixed = jnp.sum(route_affinity * scores, axis=1, keepdims=True) / score_sum
    router_grad = ROUTE_SCALE * scores * (1.0 - scores) * (route_affinity - mixed) / score_sum

    down_grad = (grad_shard / data_ways)[None]
    corr_one = 1.0 - BETA_ONE**STEP
    corr_two = 1.0 - BETA_TWO**STEP
    down_wide = down.astype(jnp.float32)
    first = BETA_ONE * moment1.astype(jnp.float32) + (1.0 - BETA_ONE) * down_grad
    second = BETA_TWO * moment2.astype(jnp.float32) + (1.0 - BETA_TWO) * down_grad * down_grad
    update = first / corr_one / (jnp.sqrt(second / corr_two) + EPSILON) + DECAY * down_wide
    new_down = (down_wide - LEARN_RATE * update).astype(jnp.bfloat16)
    return (
        token_grad,
        router_grad,
        new_down,
        first.astype(jnp.bfloat16),
        second.astype(jnp.bfloat16),
    )


def solution(mesh):
    placed = (
        P(("expert", "dp"), None),
        P(("expert", "dp"), None),
        P(("expert", "dp"), None),
        P(("expert", "dp"), None),
        P("expert", None, None, "dp"),
        P("expert", "dp", None),
        P("expert", "dp", None),
        P("expert", "dp", None),
    )
    return jax.shard_map(
        shards,
        mesh=mesh,
        in_specs=placed,
        out_specs=(
            P(("expert", "dp"), None),
            P(("expert", "dp"), None),
            P("expert", "dp", None),
            P("expert", "dp", None),
            P("expert", "dp", None),
        ),
        check_vma=False,
    )
```

```python
import jax
import jax.numpy as jnp
from jax import lax
from jax.sharding import PartitionSpec as P

STEP = 10


ROUTE_SCALE = 2.5
BETA_ONE = 0.9
BETA_TWO = 0.95
LEARN_RATE = 0.001
DECAY = 0.1
EPSILON = 1e-08


def contract_last(left, right):
    return lax.dot_general(
        left, right, (((1,), (1,)), ((), ())), preferred_element_type=jnp.float32
    )


def contract_first(left, right):
    return lax.dot_general(
        left, right, (((0,), (0,)), ((), ())), preferred_element_type=jnp.float32
    )


def shards(tokens, out_grad, route_ids, route_logits, gate_up, down, moment1, moment2):
    experts = lax.axis_size("expert")
    data_ways = lax.axis_size("dp")
    tok_rows, model_width = tokens.shape
    top_count = route_ids.shape[1]
    capacity = min(tok_rows, max(2, 5 * tok_rows * top_count // (4 * experts)))
    side_row = capacity
    capacity = -(-(capacity + 1) // 8) * 8
    slot_count = experts * capacity
    scores = jax.nn.sigmoid(route_logits)
    score_sum = jnp.sum(scores, axis=1, keepdims=True)
    route_weight = (ROUTE_SCALE * scores / score_sum).astype(jnp.bfloat16)
    flat_ids = route_ids.reshape(-1)
    onehot = (flat_ids[:, None] == jnp.arange(experts, dtype=jnp.int32)[None, :]).astype(jnp.int32)
    before = jnp.cumsum(onehot, axis=0) - onehot
    places = jnp.sum(before * onehot, axis=1)
    slot_index = flat_ids * capacity + places
    matched = (jnp.arange(slot_count, dtype=jnp.int32)[:, None] == slot_index[None, :]).astype(
        jnp.float32
    )
    tok_match = jnp.sum(matched.reshape(slot_count, tok_rows, top_count), axis=2).astype(
        jnp.bfloat16
    )
    send_weight = jnp.sum(matched * route_weight.astype(jnp.float32).reshape(-1)[None, :], axis=1)
    payload = jnp.concatenate([tokens, out_grad], axis=1)
    send_rows = jnp.dot(tok_match, payload, preferred_element_type=jnp.float32).astype(jnp.bfloat16)
    send_rows = send_rows.reshape(experts, capacity, 2 * model_width)
    send_rows = send_rows.at[:, side_row, :capacity].set(
        send_weight.astype(jnp.bfloat16).reshape(experts, capacity)
    )

    full_gu = lax.all_gather(gate_up, "dp", axis=3, tiled=True)[0]
    full_down = lax.all_gather(down, "dp", axis=1, tiled=True)[0]

    recv_rows = lax.all_to_all(send_rows, "expert", split_axis=0, concat_axis=0, tiled=True)
    slot_weight = recv_rows[:, side_row, :capacity].reshape(slot_count).astype(jnp.float32)
    recv_rows = recv_rows.reshape(slot_count, 2 * model_width)
    xs_rows = recv_rows[:, :model_width]
    gs_rows = recv_rows[:, model_width:]

    gate_w = full_gu[0]
    up_w = full_gu[1]
    pre_gate = jnp.dot(xs_rows, gate_w, preferred_element_type=jnp.float32)
    pre_up = jnp.dot(xs_rows, up_w, preferred_element_type=jnp.float32)
    sig_gate = jax.nn.sigmoid(pre_gate)
    silu_gate = pre_gate * sig_gate
    hidden = (silu_gate * pre_up).astype(jnp.bfloat16)
    scaled = (slot_weight[:, None] * gs_rows.astype(jnp.float32)).astype(jnp.bfloat16)
    local_grad = contract_first(hidden, scaled).astype(jnp.bfloat16)
    local_grad, gs_rows = lax.optimization_barrier((local_grad, gs_rows))
    grad_shard = lax.psum_scatter(local_grad, "dp", scatter_dimension=0, tiled=True).astype(
        jnp.float32
    )
    back_raw = contract_last(gs_rows, full_down)
    affinity = jnp.sum(hidden.astype(jnp.float32) * back_raw, axis=1).astype(jnp.bfloat16)
    back = slot_weight[:, None] * back_raw
    gate_grad = (back * pre_up * sig_gate * (1.0 + pre_gate * (1.0 - sig_gate))).astype(
        jnp.bfloat16
    )
    up_grad = (back * silu_gate).astype(jnp.bfloat16)
    grads = jnp.stack([gate_grad, up_grad], axis=1)
    route_in = lax.dot_general(
        grads, full_gu, (((1, 2), (0, 2)), ((), ())), preferred_element_type=jnp.float32
    ).astype(jnp.bfloat16)
    ret_rows = route_in.reshape(experts, capacity, model_width)
    ret_rows = ret_rows.at[:, side_row, :capacity].set(affinity.reshape(experts, capacity))
    back_rows = lax.all_to_all(ret_rows, "expert", split_axis=0, concat_axis=0, tiled=True)
    back_affinity = back_rows[:, side_row, :capacity].reshape(slot_count).astype(jnp.float32)
    token_grad = contract_first(tok_match, back_rows.reshape(slot_count, model_width)).astype(
        jnp.bfloat16
    )
    route_affinity = jnp.sum(matched * back_affinity[:, None], axis=0)
    route_affinity = route_affinity.reshape(tok_rows, top_count)
    mixed = jnp.sum(route_affinity * scores, axis=1, keepdims=True) / score_sum
    router_grad = ROUTE_SCALE * scores * (1.0 - scores) * (route_affinity - mixed) / score_sum

    down_grad = (grad_shard * (1.0 / data_ways))[None]
    corr_one = 1.0 - BETA_ONE**STEP
    corr_two = 1.0 - BETA_TWO**STEP
    down_wide = down.astype(jnp.float32)
    first = BETA_ONE * moment1.astype(jnp.float32) + (1.0 - BETA_ONE) * down_grad
    second = BETA_TWO * moment2.astype(jnp.float32) + (1.0 - BETA_TWO) * down_grad * down_grad
    update = (first * (1.0 / corr_one)) / (
        jnp.sqrt(second) * (1.0 / corr_two**0.5) + EPSILON
    ) + DECAY * down_wide
    new_down = (down_wide - LEARN_RATE * update).astype(jnp.bfloat16)
    return (
        token_grad,
        router_grad,
        new_down,
        first.astype(jnp.bfloat16),
        second.astype(jnp.bfloat16),
    )


def solution(mesh):
    placed = (
        P(("expert", "dp"), None),
        P(("expert", "dp"), None),
        P(("expert", "dp"), None),
        P(("expert", "dp"), None),
        P("expert", None, None, "dp"),
        P("expert", "dp", None),
        P("expert", "dp", None),
        P("expert", "dp", None),
    )
    return jax.shard_map(
        shards,
        mesh=mesh,
        in_specs=placed,
        out_specs=(
            P(("expert", "dp"), None),
            P(("expert", "dp"), None),
            P("expert", "dp", None),
            P("expert", "dp", None),
            P("expert", "dp", None),
        ),
        check_vma=False,
    )
```

```python
import jax
import jax.numpy as jnp
from jax import lax
from jax.sharding import PartitionSpec as P

STEP = 10


ROUTE_SCALE = 2.5
BETA_ONE = 0.9
BETA_TWO = 0.95
LEARN_RATE = 0.001
DECAY = 0.1
EPSILON = 1e-08


def contract_last(left, right):
    return lax.dot_general(
        left, right, (((1,), (1,)), ((), ())), preferred_element_type=jnp.float32
    )


def contract_first(left, right):
    return lax.dot_general(
        left, right, (((0,), (0,)), ((), ())), preferred_element_type=jnp.float32
    )


def shards(tokens, out_grad, route_ids, route_logits, gate_up, down, moment1, moment2):
    experts = lax.axis_size("expert")
    data_ways = lax.axis_size("dp")
    tok_rows, model_width = tokens.shape
    top_count = route_ids.shape[1]
    capacity = min(tok_rows, max(2, 5 * tok_rows * top_count // (4 * experts)))
    side_row = capacity
    capacity = -(-(capacity + 1) // 8) * 8
    slot_count = experts * capacity
    scores = jax.nn.sigmoid(route_logits)
    score_sum = jnp.sum(scores, axis=1, keepdims=True)
    route_weight = (ROUTE_SCALE * scores / score_sum).astype(jnp.bfloat16)
    flat_ids = route_ids.reshape(-1)
    onehot = (flat_ids[:, None] == jnp.arange(experts, dtype=jnp.int32)[None, :]).astype(jnp.int32)
    before = jnp.cumsum(onehot, axis=0) - onehot
    places = jnp.sum(before * onehot, axis=1)
    slot_index = flat_ids * capacity + places
    matched = (jnp.arange(slot_count, dtype=jnp.int32)[:, None] == slot_index[None, :]).astype(
        jnp.float32
    )
    tok_match = jnp.sum(matched.reshape(slot_count, tok_rows, top_count), axis=2).astype(
        jnp.bfloat16
    )
    send_weight = jnp.sum(matched * route_weight.astype(jnp.float32).reshape(-1)[None, :], axis=1)
    payload = jnp.concatenate([tokens, out_grad], axis=1)
    send_rows = jnp.dot(tok_match, payload, preferred_element_type=jnp.float32).astype(jnp.bfloat16)
    send_rows = send_rows.reshape(experts, capacity, 2 * model_width)
    send_rows = send_rows.at[:, side_row, :capacity].set(
        send_weight.astype(jnp.bfloat16).reshape(experts, capacity)
    )

    full_gu = lax.all_gather(gate_up, "dp", axis=3, tiled=True)[0]
    full_down = lax.all_gather(down, "dp", axis=1, tiled=True)[0]

    recv_rows = lax.all_to_all(send_rows, "expert", split_axis=0, concat_axis=0, tiled=True)
    slot_weight = recv_rows[:, side_row, :capacity].reshape(slot_count).astype(jnp.float32)
    recv_rows = recv_rows.reshape(slot_count, 2 * model_width)
    xs_rows = recv_rows[:, :model_width]
    gs_rows = recv_rows[:, model_width:]

    gate_w = full_gu[0]
    up_w = full_gu[1]
    pre_gate = jnp.dot(xs_rows, gate_w, preferred_element_type=jnp.float32)
    pre_up = jnp.dot(xs_rows, up_w, preferred_element_type=jnp.float32)
    sig_gate = jax.nn.sigmoid(pre_gate)
    silu_gate = pre_gate * sig_gate
    hidden = (silu_gate * pre_up).astype(jnp.bfloat16)
    scaled = (slot_weight[:, None] * gs_rows.astype(jnp.float32)).astype(jnp.bfloat16)
    local_grad = contract_first(hidden, scaled).astype(jnp.bfloat16)
    gate_factor = slot_weight[:, None] * (pre_up * sig_gate * (1.0 + pre_gate * (1.0 - sig_gate)))
    up_factor = slot_weight[:, None] * silu_gate
    factors = jnp.stack([gate_factor, up_factor], axis=1)
    local_grad, factors, gs_rows = lax.optimization_barrier((local_grad, factors, gs_rows))
    grad_shard = lax.psum_scatter(local_grad, "dp", scatter_dimension=0, tiled=True).astype(
        jnp.float32
    )
    back_raw = contract_last(gs_rows, full_down)
    affinity = jnp.sum(hidden.astype(jnp.float32) * back_raw, axis=1).astype(jnp.bfloat16)
    grads = (back_raw[:, None, :] * factors).astype(jnp.bfloat16)
    grads = lax.optimization_barrier(grads)
    route_in = lax.dot_general(
        grads, full_gu, (((1, 2), (0, 2)), ((), ())), preferred_element_type=jnp.float32
    ).astype(jnp.bfloat16)
    ret_rows = route_in.reshape(experts, capacity, model_width)
    ret_rows = ret_rows.at[:, side_row, :capacity].set(affinity.reshape(experts, capacity))
    back_rows = lax.all_to_all(ret_rows, "expert", split_axis=0, concat_axis=0, tiled=True)
    back_affinity = back_rows[:, side_row, :capacity].reshape(slot_count).astype(jnp.float32)
    token_grad = contract_first(tok_match, back_rows.reshape(slot_count, model_width)).astype(
        jnp.bfloat16
    )
    route_affinity = jnp.sum(matched * back_affinity[:, None], axis=0)
    route_affinity = route_affinity.reshape(tok_rows, top_count)
    mixed = jnp.sum(route_affinity * scores, axis=1, keepdims=True) / score_sum
    router_grad = ROUTE_SCALE * scores * (1.0 - scores) * (route_affinity - mixed) / score_sum

    down_grad = (grad_shard * (1.0 / data_ways))[None]
    corr_one = 1.0 - BETA_ONE**STEP
    corr_two = 1.0 - BETA_TWO**STEP
    down_wide = down.astype(jnp.float32)
    first = BETA_ONE * moment1.astype(jnp.float32) + (1.0 - BETA_ONE) * down_grad
    second = BETA_TWO * moment2.astype(jnp.float32) + (1.0 - BETA_TWO) * down_grad * down_grad
    update = (first * (1.0 / corr_one)) / (
        jnp.sqrt(second) * (1.0 / corr_two**0.5) + EPSILON
    ) + DECAY * down_wide
    new_down = (down_wide - LEARN_RATE * update).astype(jnp.bfloat16)
    return (
        token_grad,
        router_grad,
        new_down,
        first.astype(jnp.bfloat16),
        second.astype(jnp.bfloat16),
    )


def solution(mesh):
    placed = (
        P(("expert", "dp"), None),
        P(("expert", "dp"), None),
        P(("expert", "dp"), None),
        P(("expert", "dp"), None),
        P("expert", None, None, "dp"),
        P("expert", "dp", None),
        P("expert", "dp", None),
        P("expert", "dp", None),
    )
    return jax.shard_map(
        shards,
        mesh=mesh,
        in_specs=placed,
        out_specs=(
            P(("expert", "dp"), None),
            P(("expert", "dp"), None),
            P("expert", "dp", None),
            P("expert", "dp", None),
            P("expert", "dp", None),
        ),
        check_vma=False,
    )
```

```python
import jax
import jax.numpy as jnp
from jax import lax
from jax.sharding import PartitionSpec as P

STEP = 10


ROUTE_SCALE = 2.5
BETA_ONE = 0.9
BETA_TWO = 0.95
LEARN_RATE = 0.001
DECAY = 0.1
EPSILON = 1e-08


def contract_last(left, right):
    return lax.dot_general(
        left, right, (((1,), (1,)), ((), ())), preferred_element_type=jnp.float32
    )


def contract_first(left, right):
    return lax.dot_general(
        left, right, (((0,), (0,)), ((), ())), preferred_element_type=jnp.float32
    )


def shards(tokens, out_grad, route_ids, route_logits, gate_up, down, moment1, moment2):
    experts = lax.axis_size("expert")
    data_ways = lax.axis_size("dp")
    tok_rows, model_width = tokens.shape
    top_count = route_ids.shape[1]
    capacity = min(tok_rows, max(2, 5 * tok_rows * top_count // (4 * experts)))
    side_row = capacity
    capacity = -(-(capacity + 1) // 8) * 8
    slot_count = experts * capacity
    scores = jax.nn.sigmoid(route_logits)
    score_sum = jnp.sum(scores, axis=1, keepdims=True)
    route_weight = (ROUTE_SCALE * scores / score_sum).astype(jnp.bfloat16)
    flat_ids = route_ids.reshape(-1)
    onehot = (flat_ids[:, None] == jnp.arange(experts, dtype=jnp.int32)[None, :]).astype(jnp.int32)
    before = jnp.cumsum(onehot, axis=0) - onehot
    places = jnp.sum(before * onehot, axis=1)
    slot_index = flat_ids * capacity + places
    matched = (jnp.arange(slot_count, dtype=jnp.int32)[:, None] == slot_index[None, :]).astype(
        jnp.float32
    )
    tok_match = jnp.sum(matched.reshape(slot_count, tok_rows, top_count), axis=2).astype(
        jnp.bfloat16
    )
    send_weight = jnp.sum(matched * route_weight.astype(jnp.float32).reshape(-1)[None, :], axis=1)
    payload = jnp.concatenate([tokens, out_grad], axis=1)
    send_rows = jnp.dot(tok_match, payload, preferred_element_type=jnp.float32).astype(jnp.bfloat16)
    send_rows = send_rows.reshape(experts, capacity, 2 * model_width)
    send_rows = send_rows.at[:, side_row, :capacity].set(
        send_weight.astype(jnp.bfloat16).reshape(experts, capacity)
    )

    full_gu = lax.all_gather(gate_up, "dp", axis=3, tiled=True)[0]
    full_down = lax.all_gather(down, "dp", axis=1, tiled=True)[0]

    recv_rows = lax.all_to_all(send_rows, "expert", split_axis=0, concat_axis=0, tiled=True)
    slot_weight = recv_rows[:, side_row, :capacity].reshape(slot_count).astype(jnp.float32)
    recv_rows = recv_rows.reshape(slot_count, 2 * model_width)
    xs_rows = recv_rows[:, :model_width]
    gs_rows = recv_rows[:, model_width:]

    gate_w = full_gu[0]
    up_w = full_gu[1]
    pre_gate = jnp.dot(xs_rows, gate_w, preferred_element_type=jnp.float32)
    pre_up = jnp.dot(xs_rows, up_w, preferred_element_type=jnp.float32)
    sig_gate = jax.nn.sigmoid(pre_gate)
    silu_gate = pre_gate * sig_gate
    hidden = (silu_gate * pre_up).astype(jnp.bfloat16)
    scaled = (slot_weight[:, None] * gs_rows.astype(jnp.float32)).astype(jnp.bfloat16)
    local_grad = contract_first(hidden, scaled).astype(jnp.bfloat16)
    local_grad, gs_rows = lax.optimization_barrier((local_grad, gs_rows))
    grad_shard = lax.psum_scatter(local_grad, "dp", scatter_dimension=0, tiled=True).astype(
        jnp.float32
    )
    back_raw = contract_last(gs_rows, full_down)
    affinity = jnp.sum(hidden.astype(jnp.float32) * back_raw, axis=1).astype(jnp.bfloat16)
    back = slot_weight[:, None] * back_raw
    gate_grad = (back * pre_up * sig_gate * (1.0 + pre_gate * (1.0 - sig_gate))).astype(
        jnp.bfloat16
    )
    up_grad = (back * silu_gate).astype(jnp.bfloat16)
    grads = jnp.stack([gate_grad, up_grad], axis=1)
    route_in = lax.dot_general(
        grads, full_gu, (((1, 2), (0, 2)), ((), ())), preferred_element_type=jnp.float32
    ).astype(jnp.bfloat16)
    ret_rows = route_in.reshape(experts, capacity, model_width)
    ret_rows = ret_rows.at[:, side_row, :capacity].set(affinity.reshape(experts, capacity))
    back_rows = lax.all_to_all(ret_rows, "expert", split_axis=0, concat_axis=0, tiled=True)
    down_grad = (grad_shard * (1.0 / data_ways))[None]
    corr_one = 1.0 - BETA_ONE**STEP
    corr_two = 1.0 - BETA_TWO**STEP
    down_wide = down.astype(jnp.float32)
    first = BETA_ONE * moment1.astype(jnp.float32) + (1.0 - BETA_ONE) * down_grad
    second = BETA_TWO * moment2.astype(jnp.float32) + (1.0 - BETA_TWO) * down_grad * down_grad
    update = (first * (1.0 / corr_one)) / (
        jnp.sqrt(second) * (1.0 / corr_two**0.5) + EPSILON
    ) + DECAY * down_wide
    new_down = (down_wide - LEARN_RATE * update).astype(jnp.bfloat16)
    back_rows, new_down, first, second = lax.optimization_barrier((back_rows, new_down, first, second))
    back_affinity = back_rows[:, side_row, :capacity].reshape(slot_count).astype(jnp.float32)
    token_grad = contract_first(tok_match, back_rows.reshape(slot_count, model_width)).astype(
        jnp.bfloat16
    )
    route_affinity = jnp.sum(matched * back_affinity[:, None], axis=0)
    route_affinity = route_affinity.reshape(tok_rows, top_count)
    mixed = jnp.sum(route_affinity * scores, axis=1, keepdims=True) / score_sum
    router_grad = ROUTE_SCALE * scores * (1.0 - scores) * (route_affinity - mixed) / score_sum

    return (
        token_grad,
        router_grad,
        new_down,
        first.astype(jnp.bfloat16),
        second.astype(jnp.bfloat16),
    )


def solution(mesh):
    placed = (
        P(("expert", "dp"), None),
        P(("expert", "dp"), None),
        P(("expert", "dp"), None),
        P(("expert", "dp"), None),
        P("expert", None, None, "dp"),
        P("expert", "dp", None),
        P("expert", "dp", None),
        P("expert", "dp", None),
    )
    return jax.shard_map(
        shards,
        mesh=mesh,
        in_specs=placed,
        out_specs=(
            P(("expert", "dp"), None),
            P(("expert", "dp"), None),
            P("expert", "dp", None),
            P("expert", "dp", None),
            P("expert", "dp", None),
        ),
        check_vma=False,
    )
```
